512 devices in a mesh: mem: 128 (over z, y, core), dom: 4 (over x).
Axes of the slice: x: 4, y: 8, z: 8, core: 2. Of those that a mesh axis runs over, the one named last changes fastest.
Arguments:
- fcst_pert: float32 [2, 1024, 4, 16384], P(None, 'mem', 'dom'), may hold values from -6 to 6
- sensitivity: float32 [2, 64, 4, 16384], P(None, None, 'dom', 'mem'), may hold values from -6 to 6
- obs_pert: float32 [393216, 1024], P(('mem', 'dom')), may hold values from -6 to 6
- weighted_innovation: float32 [393216], P(('mem', 'dom')), may hold values from -8 to 8
- obs_lists: int32 [128, 16], replicated, may hold values from 0 to 3071, as said below
- block_taper: float32 [128, 16], replicated, may hold values from 0.2 to 1
- counts: int32 [128], replicated, may hold values from 8 to 16, as said below
Outputs:
- impact: float32 [393216, 128], P(('mem', 'dom'))
The draws below stay inside these ranges and needn't reach their ends.
Inputs may be any that keep to these rules, and one draw needn't show every extreme that they name: `obs_lists`: each row's ids are distinct, and every id names an observation block whose column block is within one of the row's column block, cyclically. Observation block o belongs to column block o // 24 and region (o // 6) % 4. The first 8 slots of each row name, for every region, one block of the column block before and one of the column block after. `counts`: some column block uses all 16 slots.
All inputs are finite; a program needn't handle non-finite values.
Results may differ from the reference program's by a relative error of at most 0.0003.
Values sent between devices are 32-bit elements; how exact they have to be, the bound alone decides.
No kernel may reach another device: no remote copies, remote signals or barrier semaphores. Data moves between devices by JAX's collectives and lax.ppermute only.
A program may use at most 128 MiB of HBM per device.

```python
import jax
import jax.numpy as jnp
from jax import lax

M = 1024
T_SIZE = 64
LEADS = 2
OBSB = 128
LMAX = 16
BLK_DEV = 6
COL_DEV = 128
REGIONS = 4
CBLK = 128
LEV = 4
COLS = 16384
OBLK = 3072
OBS = 393216


def draw_obs_lists(key, part):
    candidates = 3 * REGIONS * BLK_DEV
    list_key = jax.random.fold_in(key, 11)
    inner_key, order_key = jax.random.split(list_key)
    chosen_inner = jax.random.randint(inner_key, (CBLK, 3, REGIONS), 0, BLK_DEV, dtype=jnp.int32)
    cand = jnp.arange(candidates, dtype=jnp.int32)
    cand_offset = cand // (REGIONS * BLK_DEV)
    cand_region = cand // BLK_DEV % REGIONS
    cand_inner = cand % BLK_DEV
    picked_inner = chosen_inner[:, cand_offset, cand_region]
    forced = (cand_offset[None, :] != 1) & (cand_inner[None, :] == picked_inner)
    row_keys = jax.random.split(order_key, CBLK)
    perms = jax.vmap(lambda one_key: jax.random.permutation(one_key, candidates))(row_keys).astype(jnp.int32)
    scores = jnp.where(forced, perms, perms + candidates)
    order = jnp.argsort(scores, axis=1, stable=True).astype(jnp.int32)
    picks = order[:, :LMAX]
    offsets = picks // (REGIONS * BLK_DEV) - 1
    region_ids = picks // BLK_DEV % REGIONS
    inner_ids = picks % BLK_DEV
    column_ids = (jnp.arange(CBLK, dtype=jnp.int32)[:, None] + offsets) % CBLK
    return ((column_ids * REGIONS + region_ids) * BLK_DEV + inner_ids).astype(jnp.int32)


def draw_counts(key, part):
    count_key, place_key = jax.random.split(jax.random.fold_in(key, 23))
    drawn = jax.random.randint(count_key, (CBLK,), 2 * REGIONS, LMAX + 1, dtype=jnp.int32)
    fullest = jax.random.randint(place_key, (), 0, CBLK, dtype=jnp.int32)
    return drawn.at[fullest].set(LMAX).astype(jnp.int32)


def block_levels(stream_key, dims, cuts, low, largest):
    gain, own = 1.0, jax.random.fold_in(stream_key, 6)
    for position, blocks in cuts:
        steps = jnp.exp(jax.random.uniform(jax.random.fold_in(own, position), (blocks,), jnp.float32, low / len(cuts), largest / len(cuts)))
        gain = gain * jnp.repeat(steps, dims[position] // blocks).reshape([-1 if axis == position else 1 for axis in range(len(dims))])
    return gain


def gaussian(rng, dims, width, reach, shards=(), kind=jnp.bfloat16):
    values = width * jax.random.normal(rng, dims, jnp.float32)
    if shards:
        values = values * block_levels(rng, dims, shards, -0.22, 0.18)
    return jnp.clip(values, -reach, reach).astype(kind)


def setup_inputs(seed: int = 0) -> dict:
    key_list = jax.random.split(jax.random.key(seed), 8)
    fcst_pert = gaussian(key_list[0], (LEADS, M, LEV, COLS), 1.0, 6.0, ((1, 128), (2, 4)), jnp.float32)
    sensitivity = gaussian(key_list[1], (LEADS, T_SIZE, LEV, COLS), 1.0, 6.0, ((2, 4), (3, 128)), jnp.float32)
    obs_pert = gaussian(key_list[2], (OBS, M), 1.0, 6.0, ((0, 512),), jnp.float32)
    weighted_innovation = gaussian(key_list[3], (OBS,), 1.5, 8.0, ((0, 512),), jnp.float32)
    obs_lists = draw_obs_lists(jax.random.fold_in(key_list[7], 71), 0)
    block_taper = jnp.clip(jax.random.uniform(key_list[5], (CBLK, LMAX), jnp.float32, 0.2, 1.0), 0.2, 1.0)
    counts = draw_counts(jax.random.fold_in(key_list[7], 71), 0)
    return {"fcst_pert": fcst_pert, "sensitivity": sensitivity, "obs_pert": obs_pert, "weighted_innovation": weighted_innovation, "obs_lists": obs_lists, "block_taper": block_taper, "counts": counts}


def reference(fcst_pert, sensitivity, obs_pert, weighted_innovation, obs_lists, block_taper, counts):
    grid_x = fcst_pert.reshape(LEADS, M, LEV, CBLK, COL_DEV)
    grid_s = sensitivity.reshape(LEADS, T_SIZE, LEV, CBLK, COL_DEV)

    def column_sums(index):
        xpart = lax.dynamic_index_in_dim(grid_x, index, 3, keepdims=False)
        spart = lax.dynamic_index_in_dim(grid_s, index, 3, keepdims=False)
        summed = jnp.einsum('lkvc,ltvc->klt', xpart, spart, precision=lax.Precision.HIGHEST)
        return summed.reshape(M, LEADS * T_SIZE)

    contracted = lax.map(column_sums, jnp.arange(CBLK, dtype=jnp.int32))
    slot_live = jnp.arange(LMAX, dtype=jnp.int32)[None, :] < counts[:, None]
    matches = (obs_lists[:, :, None] == jnp.arange(OBLK, dtype=jnp.int32)[None, None, :]) & slot_live[:, :, None]
    weights = jnp.sum(jnp.where(matches, block_taper[:, :, None], jnp.zeros((), block_taper.dtype)), axis=1)
    obs_blocks = obs_pert.reshape(OBLK, OBSB, M)
    innov_blocks = weighted_innovation.reshape(OBLK, OBSB)

    def block_impact(index):
        column = index // (REGIONS * BLK_DEV)
        sources = ((column + jnp.arange(3, dtype=jnp.int32) - 1) % CBLK).astype(jnp.int32)
        source_weights = weights[sources, index]
        source_sums = contracted[sources]
        combined = jnp.einsum('s,skt->kt', source_weights, source_sums, precision=lax.Precision.HIGHEST)
        result = jnp.dot(obs_blocks[index], combined, precision=lax.Precision.HIGHEST)
        return result * (innov_blocks[index] / (M - 1))[:, None]

    impact = lax.map(block_impact, jnp.arange(OBLK, dtype=jnp.int32))
    return impact.reshape(OBS, LEADS * T_SIZE)
```

```python
import jax
import jax.numpy as jnp
from jax import lax
from jax.sharding import PartitionSpec as P

M = 1024
OBSB = 128
HIGHEST = lax.Precision.HIGHEST


def from_behind(block, axis, distance):
    devices = range(lax.axis_size(axis))
    route = [((i - distance) % len(devices), i) for i in devices]
    return lax.ppermute(block, axis, route)


def own_weights(obs_lists, block_taper, counts, column_index, region_index, owned_blocks, regions):
    column_count, slots = obs_lists.shape
    rows = (column_index + jnp.arange(3, dtype=jnp.int32) - 1) % column_count
    row_ids = obs_lists[rows]
    row_taper = block_taper[rows]
    row_count = counts[rows]
    slot_live = jnp.arange(slots, dtype=jnp.int32)[None, :] < row_count[:, None]
    own_ids = (column_index * regions + region_index) * owned_blocks + jnp.arange(
        owned_blocks, dtype=jnp.int32
    )
    matched = (row_ids[:, None, :] == own_ids[None, :, None]) & slot_live[:, None, :]
    return jnp.sum(
        jnp.where(matched, row_taper[:, None, :], jnp.zeros((), row_taper.dtype)), axis=2
    )


def body(fcst_pert, sensitivity, obs_pert, weighted_innovation, obs_lists, block_taper, counts):
    leads, local_members, _, columns = fcst_pert.shape
    column_blocks = lax.axis_size("mem")
    width = columns // column_blocks
    grid = fcst_pert.reshape(leads, local_members, column_blocks, width)
    grid = jnp.transpose(grid, (2, 0, 1, 3))
    regrouped = lax.all_to_all(grid, "mem", 0, 0, tiled=True)
    targets = sensitivity.shape[1]
    per_lead = []
    for lead in range(leads):
        left = regrouped[:, lead].reshape(-1, width)
        right = sensitivity[lead].reshape(targets, width)
        per_lead.append(
            lax.dot_general(left, right, (((1,), (1,)), ((), ())), precision=HIGHEST)
        )
    partial_sums = jnp.concatenate(per_lead, axis=1)
    summed = lax.psum(partial_sums, "dom")
    regions = lax.axis_size("dom")
    column_index = lax.axis_index("mem")
    region_index = lax.axis_index("dom")
    owned_rows = obs_pert.shape[0]
    owned_blocks = owned_rows // OBSB
    sources = (from_behind(summed, "mem", 1), summed, from_behind(summed, "mem", -1))
    weight_rows = own_weights(
        obs_lists, block_taper, counts, column_index, region_index, owned_blocks, regions
    )
    combined = sum(
        weight_rows[s][:, None, None] * sources[s][None] for s in range(len(sources))
    )
    rows = obs_pert.reshape(owned_blocks, OBSB, -1)
    result = jnp.einsum("irk,ikt->irt", rows, combined, precision=HIGHEST)
    result = result.reshape(owned_rows, -1)
    return result * (weighted_innovation / (M - 1))[:, None]


def solution(mesh):
    in_specs = (
        P(None, "mem", "dom", None),
        P(None, None, "dom", "mem"),
        P(("mem", "dom"), None),
        P(("mem", "dom")),
        P(),
        P(),
        P(),
    )
    out_specs = P(("mem", "dom"), None)
    return jax.shard_map(body, mesh=mesh, in_specs=in_specs, out_specs=out_specs, check_vma=False)
```

```python
import jax
import jax.numpy as jnp
from jax import lax
from jax.sharding import PartitionSpec as P

M = 1024
OBSB = 128
HIGHEST = lax.Precision.HIGHEST


def from_behind(block, axis, distance):
    devices = range(lax.axis_size(axis))
    route = [((i - distance) % len(devices), i) for i in devices]
    return lax.ppermute(block, axis, route)


def gathered_sum(partial, axis):
    count = lax.axis_size(axis)
    pieces = partial.reshape(count, partial.shape[0] // count, partial.shape[1])
    owned = lax.all_to_all(pieces, axis, 0, 0, tiled=True).sum(axis=0)
    copies = jnp.broadcast_to(owned[None], (count,) + owned.shape)
    return lax.all_to_all(copies, axis, 0, 0, tiled=True).reshape(partial.shape)


def own_weights(obs_lists, block_taper, counts, column_index, region_index, owned_blocks, regions):
    column_count, slots = obs_lists.shape
    rows = (column_index + jnp.arange(3, dtype=jnp.int32) - 1) % column_count
    row_ids = obs_lists[rows]
    row_taper = block_taper[rows]
    row_count = counts[rows]
    slot_live = jnp.arange(slots, dtype=jnp.int32)[None, :] < row_count[:, None]
    own_ids = (column_index * regions + region_index) * owned_blocks + jnp.arange(
        owned_blocks, dtype=jnp.int32
    )
    matched = (row_ids[:, None, :] == own_ids[None, :, None]) & slot_live[:, None, :]
    return jnp.sum(
        jnp.where(matched, row_taper[:, None, :], jnp.zeros((), row_taper.dtype)), axis=2
    )


def body(fcst_pert, sensitivity, obs_pert, weighted_innovation, obs_lists, block_taper, counts):
    leads, local_members, _, columns = fcst_pert.shape
    column_blocks = lax.axis_size("mem")
    width = columns // column_blocks
    grid = fcst_pert.reshape(leads, local_members, column_blocks, width)
    grid = jnp.transpose(grid, (2, 0, 1, 3))
    regrouped = lax.all_to_all(grid, "mem", 0, 0, tiled=True)
    targets = sensitivity.shape[1]
    per_lead = []
    for lead in range(leads):
        left = regrouped[:, lead].reshape(-1, width)
        right = sensitivity[lead].reshape(targets, width)
        per_lead.append(
            lax.dot_general(left, right, (((1,), (1,)), ((), ())), precision=HIGHEST)
        )
    partial_sums = jnp.concatenate(per_lead, axis=1)
    summed = gathered_sum(partial_sums, "dom")
    regions = lax.axis_size("dom")
    column_index = lax.axis_index("mem")
    region_index = lax.axis_index("dom")
    owned_rows = obs_pert.shape[0]
    owned_blocks = owned_rows // OBSB
    sources = (from_behind(summed, "mem", 1), summed, from_behind(summed, "mem", -1))
    weight_rows = own_weights(
        obs_lists, block_taper, counts, column_index, region_index, owned_blocks, regions
    )
    combined = sum(
        weight_rows[s][:, None, None] * sources[s][None] for s in range(len(sources))
    )
    rows = obs_pert.reshape(owned_blocks, OBSB, -1)
    result = jnp.einsum("irk,ikt->irt", rows, combined, precision=HIGHEST)
    result = result.reshape(owned_rows, -1)
    return result * (weighted_innovation / (M - 1))[:, None]


def solution(mesh):
    in_specs = (
        P(None, "mem", "dom", None),
        P(None, None, "dom", "mem"),
        P(("mem", "dom"), None),
        P(("mem", "dom")),
        P(),
        P(),
        P(),
    )
    out_specs = P(("mem", "dom"), None)
    return jax.shard_map(body, mesh=mesh, in_specs=in_specs, out_specs=out_specs, check_vma=False)
```

```python
import jax
import jax.numpy as jnp
from jax import lax
from jax.sharding import PartitionSpec as P

M = 1024
OBSB = 128
HIGH = lax.Precision.HIGH


def from_behind(block, axis, distance):
    devices = range(lax.axis_size(axis))
    route = [((i - distance) % len(devices), i) for i in devices]
    return lax.ppermute(block, axis, route)


def gathered_sum(partial, axis):
    count = lax.axis_size(axis)
    pieces = partial.reshape(count, partial.shape[0] // count, partial.shape[1])
    owned = lax.all_to_all(pieces, axis, 0, 0, tiled=True).sum(axis=0)
    copies = jnp.broadcast_to(owned[None], (count,) + owned.shape)
    return lax.all_to_all(copies, axis, 0, 0, tiled=True).reshape(partial.shape)


def own_weights(obs_lists, block_taper, counts, column_index, region_index, owned_blocks, regions):
    column_count, slots = obs_lists.shape
    rows = (column_index + jnp.arange(3, dtype=jnp.int32) - 1) % column_count
    row_ids = obs_lists[rows]
    row_taper = block_taper[rows]
    row_count = counts[rows]
    slot_live = jnp.arange(slots, dtype=jnp.int32)[None, :] < row_count[:, None]
    own_ids = (column_index * regions + region_index) * owned_blocks + jnp.arange(
        owned_blocks, dtype=jnp.int32
    )
    matched = (row_ids[:, None, :] == own_ids[None, :, None]) & slot_live[:, None, :]
    return jnp.sum(
        jnp.where(matched, row_taper[:, None, :], jnp.zeros((), row_taper.dtype)), axis=2
    )


def body(fcst_pert, sensitivity, obs_pert, weighted_innovation, obs_lists, block_taper, counts):
    leads, local_members, _, columns = fcst_pert.shape
    column_blocks = lax.axis_size("mem")
    width = columns // column_blocks
    grid = fcst_pert.reshape(leads, local_members, column_blocks, width)
    grid = jnp.transpose(grid, (2, 0, 1, 3))
    regrouped = lax.all_to_all(grid, "mem", 0, 0, tiled=True)
    targets = sensitivity.shape[1]
    per_lead = []
    for lead in range(leads):
        left = regrouped[:, lead].reshape(-1, width)
        right = sensitivity[lead].reshape(targets, width)
        per_lead.append(
            lax.dot_general(left, right, (((1,), (1,)), ((), ())), precision=HIGH)
        )
    partial_sums = jnp.concatenate(per_lead, axis=1)
    summed = gathered_sum(partial_sums, "dom")
    regions = lax.axis_size("dom")
    column_index = lax.axis_index("mem")
    region_index = lax.axis_index("dom")
    owned_rows = obs_pert.shape[0]
    owned_blocks = owned_rows // OBSB
    sources = (from_behind(summed, "mem", 1), summed, from_behind(summed, "mem", -1))
    weight_rows = own_weights(
        obs_lists, block_taper, counts, column_index, region_index, owned_blocks, regions
    )
    combined = sum(
        weight_rows[s][:, None, None] * sources[s][None] for s in range(len(sources))
    )
    rows = obs_pert.reshape(owned_blocks, OBSB, -1)
    result = jnp.einsum("irk,ikt->irt", rows, combined, precision=HIGH)
    result = result.reshape(owned_rows, -1)
    return result * (weighted_innovation / (M - 1))[:, None]


def solution(mesh):
    in_specs = (
        P(None, "mem", "dom", None),
        P(None, None, "dom", "mem"),
        P(("mem", "dom"), None),
        P(("mem", "dom")),
        P(),
        P(),
        P(),
    )
    out_specs = P(("mem", "dom"), None)
    return jax.shard_map(body, mesh=mesh, in_specs=in_specs, out_specs=out_specs, check_vma=False)
```

```python
import jax
import jax.numpy as jnp
from jax import lax
from jax.sharding import PartitionSpec as P

M = 1024
OBSB = 128
HIGH = lax.Precision.HIGH


def from_behind(block, axis, distance):
    devices = range(lax.axis_size(axis))
    route = [((i - distance) % len(devices), i) for i in devices]
    return lax.ppermute(block, axis, route)


def gathered(piece, axis):
    count = lax.axis_size(axis)
    copies = jnp.broadcast_to(piece[None], (count,) + piece.shape)
    return lax.all_to_all(copies, axis, 0, 0, tiled=True)


def own_weights(obs_lists, block_taper, counts, column_index, region_index, owned_blocks, regions):
    column_count, slots = obs_lists.shape
    rows = (column_index + jnp.arange(3, dtype=jnp.int32) - 1) % column_count
    row_ids = obs_lists[rows]
    row_taper = block_taper[rows]
    row_count = counts[rows]
    slot_live = jnp.arange(slots, dtype=jnp.int32)[None, :] < row_count[:, None]
    own_ids = (column_index * regions + region_index) * owned_blocks + jnp.arange(
        owned_blocks, dtype=jnp.int32
    )
    matched = (row_ids[:, None, :] == own_ids[None, :, None]) & slot_live[:, None, :]
    return jnp.sum(
        jnp.where(matched, row_taper[:, None, :], jnp.zeros((), row_taper.dtype)), axis=2
    )


def body(fcst_pert, sensitivity, obs_pert, weighted_innovation, obs_lists, block_taper, counts):
    leads, local_members, _, columns = fcst_pert.shape
    column_blocks = lax.axis_size("mem")
    regions = lax.axis_size("dom")
    width = columns // column_blocks
    pair = local_members // regions
    grid = fcst_pert.reshape(leads, regions, pair, column_blocks, width)
    grid = jnp.transpose(grid, (3, 1, 0, 2, 4)).reshape(column_blocks * regions, -1)
    arrived = lax.all_to_all(grid, ("mem", "dom"), 0, 0, tiled=True)
    arrived = arrived.reshape(column_blocks, regions, leads, pair, width)
    targets = sensitivity.shape[1]
    levels = gathered(sensitivity[:, :, 0, :], "dom")
    quarter = jnp.einsum("mdljc,dltc->mjlt", arrived, levels, precision=HIGH)
    quarter = quarter.reshape(column_blocks * pair, leads * targets)
    full = gathered(quarter, "dom").reshape(regions, column_blocks, pair, -1)
    summed = jnp.transpose(full, (1, 0, 2, 3)).reshape(column_blocks * local_members, -1)
    column_index = lax.axis_index("mem")
    region_index = lax.axis_index("dom")
    owned_rows = obs_pert.shape[0]
    owned_blocks = owned_rows // OBSB
    sources = (from_behind(summed, "mem", 1), summed, from_behind(summed, "mem", -1))
    weight_rows = own_weights(
        obs_lists, block_taper, counts, column_index, region_index, owned_blocks, regions
    )
    combined = sum(
        weight_rows[s][:, None, None] * sources[s][None] for s in range(len(sources))
    )
    rows = obs_pert.reshape(owned_blocks, OBSB, -1)
    result = jnp.einsum("irk,ikt->irt", rows, combined, precision=HIGH)
    result = result.reshape(owned_rows, -1)
    return result * (weighted_innovation / (M - 1))[:, None]


def solution(mesh):
    in_specs = (
        P(None, "mem", "dom", None),
        P(None, None, "dom", "mem"),
        P(("mem", "dom"), None),
        P(("mem", "dom")),
        P(),
        P(),
        P(),
    )
    out_specs = P(("mem", "dom"), None)
    return jax.shard_map(body, mesh=mesh, in_specs=in_specs, out_specs=out_specs, check_vma=False)
```

```python
import jax
import jax.numpy as jnp
from jax import lax
from jax.sharding import PartitionSpec as P

M = 1024
OBSB = 128
HIGH = lax.Precision.HIGH


def from_behind(block, axis, distance):
    devices = range(lax.axis_size(axis))
    route = [((i - distance) % len(devices), i) for i in devices]
    return lax.ppermute(block, axis, route)


def gathered(piece, axis):
    count = lax.axis_size(axis)
    copies = jnp.broadcast_to(piece[None], (count,) + piece.shape)
    return lax.all_to_all(copies, axis, 0, 0, tiled=True)


def shifted_copies(piece, axis):
    count = lax.axis_size(axis)
    index = lax.axis_index(axis)
    arrived = [piece] + [from_behind(piece, axis, step) for step in range(1, count)]
    order = (index - jnp.arange(count, dtype=jnp.int32)) % count
    slots = jnp.zeros((count,) + piece.shape, piece.dtype)
    return slots.at[order].set(jnp.stack(arrived))


def own_weights(obs_lists, block_taper, counts, column_index, region_index, owned_blocks, regions):
    column_count, slots = obs_lists.shape
    rows = (column_index + jnp.arange(3, dtype=jnp.int32) - 1) % column_count
    row_ids = obs_lists[rows]
    row_taper = block_taper[rows]
    row_count = counts[rows]
    slot_live = jnp.arange(slots, dtype=jnp.int32)[None, :] < row_count[:, None]
    own_ids = (column_index * regions + region_index) * owned_blocks + jnp.arange(
        owned_blocks, dtype=jnp.int32
    )
    matched = (row_ids[:, None, :] == own_ids[None, :, None]) & slot_live[:, None, :]
    return jnp.sum(
        jnp.where(matched, row_taper[:, None, :], jnp.zeros((), row_taper.dtype)), axis=2
    )


def body(fcst_pert, sensitivity, obs_pert, weighted_innovation, obs_lists, block_taper, counts):
    leads, local_members, _, columns = fcst_pert.shape
    column_blocks = lax.axis_size("mem")
    regions = lax.axis_size("dom")
    width = columns // column_blocks
    pair = local_members // regions
    grid = fcst_pert.reshape(leads, regions, pair, column_blocks, width)
    grid = jnp.transpose(grid, (3, 1, 0, 2, 4)).reshape(column_blocks * regions, -1)
    arrived = lax.all_to_all(grid, ("mem", "dom"), 0, 0, tiled=True)
    arrived = arrived.reshape(column_blocks, regions, leads, pair, width)
    targets = sensitivity.shape[1]
    levels = shifted_copies(sensitivity[:, :, 0, :], "dom")
    quarter = jnp.einsum("mdljc,dltc->mjlt", arrived, levels, precision=HIGH)
    quarter = quarter.reshape(column_blocks * pair, leads * targets)
    full = gathered(quarter, "dom").reshape(regions, column_blocks, pair, -1)
    summed = jnp.transpose(full, (1, 0, 2, 3)).reshape(column_blocks * local_members, -1)
    column_index = lax.axis_index("mem")
    region_index = lax.axis_index("dom")
    owned_rows = obs_pert.shape[0]
    owned_blocks = owned_rows // OBSB
    sources = (from_behind(summed, "mem", 1), summed, from_behind(summed, "mem", -1))
    weight_rows = own_weights(
        obs_lists, block_taper, counts, column_index, region_index, owned_blocks, regions
    )
    combined = sum(
        weight_rows[s][:, None, None] * sources[s][None] for s in range(len(sources))
    )
    rows = obs_pert.reshape(owned_blocks, OBSB, -1)
    result = jnp.einsum("irk,ikt->irt", rows, combined, precision=HIGH)
    result = result.reshape(owned_rows, -1)
    return result * (weighted_innovation / (M - 1))[:, None]


def solution(mesh):
    in_specs = (
        P(None, "mem", "dom", None),
        P(None, None, "dom", "mem"),
        P(("mem", "dom"), None),
        P(("mem", "dom")),
        P(),
        P(),
        P(),
    )
    out_specs = P(("mem", "dom"), None)
    return jax.shard_map(body, mesh=mesh, in_specs=in_specs, out_specs=out_specs, check_vma=False)
```

```python
import jax
import jax.numpy as jnp
from jax import lax
from jax.sharding import PartitionSpec as P

M = 1024
OBSB = 128
HIGH = lax.Precision.HIGH


def from_behind(block, axis, distance):
    devices = range(lax.axis_size(axis))
    route = [((i - distance) % len(devices), i) for i in devices]
    return lax.ppermute(block, axis, route)


def gathered(piece, axis):
    count = lax.axis_size(axis)
    copies = jnp.broadcast_to(piece[None], (count,) + piece.shape)
    return lax.all_to_all(copies, axis, 0, 0, tiled=True)


def shifted_copies(piece, axis):
    count = lax.axis_size(axis)
    index = lax.axis_index(axis)
    arrived = [piece] + [from_behind(piece, axis, step) for step in range(1, count)]
    order = (index - jnp.arange(count, dtype=jnp.int32)) % count
    slots = jnp.zeros((count,) + piece.shape, piece.dtype)
    return slots.at[order].set(jnp.stack(arrived))


def own_weights(obs_lists, block_taper, counts, column_index, region_index, owned_blocks, regions):
    column_count, slots = obs_lists.shape
    rows = (column_index + jnp.arange(3, dtype=jnp.int32) - 1) % column_count
    row_ids = obs_lists[rows]
    row_taper = block_taper[rows]
    row_count = counts[rows]
    slot_live = jnp.arange(slots, dtype=jnp.int32)[None, :] < row_count[:, None]
    own_ids = (column_index * regions + region_index) * owned_blocks + jnp.arange(
        owned_blocks, dtype=jnp.int32
    )
    matched = (row_ids[:, None, :] == own_ids[None, :, None]) & slot_live[:, None, :]
    return jnp.sum(
        jnp.where(matched, row_taper[:, None, :], jnp.zeros((), row_taper.dtype)), axis=2
    )


def body(fcst_pert, sensitivity, obs_pert, weighted_innovation, obs_lists, block_taper, counts):
    leads, local_members, _, columns = fcst_pert.shape
    column_blocks = lax.axis_size("mem")
    regions = lax.axis_size("dom")
    width = columns // column_blocks
    pair = local_members // regions
    grid = fcst_pert.reshape(leads, regions, pair, column_blocks, width)
    grid = jnp.transpose(grid, (3, 1, 0, 2, 4)).reshape(column_blocks * regions, -1)
    arrived = lax.all_to_all(grid, ("mem", "dom"), 0, 0, tiled=True)
    arrived = arrived.reshape(column_blocks, regions, leads, pair, width)
    targets = sensitivity.shape[1]
    levels = shifted_copies(sensitivity[:, :, 0, :], "dom")
    quarter = jnp.einsum("mdljc,dltc->mjlt", arrived, levels, precision=HIGH)
    quarter = quarter.reshape(column_blocks * pair, leads * targets)
    trio = jnp.stack([from_behind(quarter, "mem", 1), quarter, from_behind(quarter, "mem", -1)])
    full = gathered(trio, "dom").reshape(regions, len(trio), column_blocks, pair, -1)
    full = jnp.transpose(full, (1, 2, 0, 3, 4)).reshape(len(trio), column_blocks * local_members, -1)
    column_index = lax.axis_index("mem")
    region_index = lax.axis_index("dom")
    owned_rows = obs_pert.shape[0]
    owned_blocks = owned_rows // OBSB
    sources = [full[s] for s in range(len(trio))]
    weight_rows = own_weights(
        obs_lists, block_taper, counts, column_index, region_index, owned_blocks, regions
    )
    combined = sum(
        weight_rows[s][:, None, None] * sources[s][None] for s in range(len(sources))
    )
    rows = obs_pert.reshape(owned_blocks, OBSB, -1)
    result = jnp.einsum("irk,ikt->irt", rows, combined, precision=HIGH)
    result = result.reshape(owned_rows, -1)
    return result * (weighted_innovation / (M - 1))[:, None]


def solution(mesh):
    in_specs = (
        P(None, "mem", "dom", None),
        P(None, None, "dom", "mem"),
        P(("mem", "dom"), None),
        P(("mem", "dom")),
        P(),
        P(),
        P(),
    )
    out_specs = P(("mem", "dom"), None)
    return jax.shard_map(body, mesh=mesh, in_specs=in_specs, out_specs=out_specs, check_vma=False)
```

```python
import jax
import jax.numpy as jnp
from jax import lax
from jax.sharding import PartitionSpec as P

M = 1024
OBSB = 128
HIGH = lax.Precision.HIGH


def from_behind(block, axis, distance):
    devices = range(lax.axis_size(axis))
    route = [((i - distance) % len(devices), i) for i in devices]
    return lax.ppermute(block, axis, route)


def gathered(piece, axis):
    count = lax.axis_size(axis)
    copies = jnp.broadcast_to(piece[None], (count,) + piece.shape)
    return lax.all_to_all(copies, axis, 0, 0, tiled=True)


def shifted_copies(piece, axis):
    count = lax.axis_size(axis)
    index = lax.axis_index(axis)
    arrived = [piece] + [from_behind(piece, axis, step) for step in range(1, count)]
    order = (index - jnp.arange(count, dtype=jnp.int32)) % count
    slots = jnp.zeros((count,) + piece.shape, piece.dtype)
    return slots.at[order].set(jnp.stack(arrived))


def own_weights(obs_lists, block_taper, counts, column_index, region_index, owned_blocks, regions):
    column_count, slots = obs_lists.shape
    rows = (column_index + jnp.arange(3, dtype=jnp.int32) - 1) % column_count
    row_ids = obs_lists[rows]
    row_taper = block_taper[rows]
    row_count = counts[rows]
    slot_live = jnp.arange(slots, dtype=jnp.int32)[None, :] < row_count[:, None]
    own_ids = (column_index * regions + region_index) * owned_blocks + jnp.arange(
        owned_blocks, dtype=jnp.int32
    )
    matched = (row_ids[:, None, :] == own_ids[None, :, None]) & slot_live[:, None, :]
    return jnp.sum(
        jnp.where(matched, row_taper[:, None, :], jnp.zeros((), row_taper.dtype)), axis=2
    )


def body(fcst_pert, sensitivity, obs_pert, weighted_innovation, obs_lists, block_taper, counts):
    leads, local_members, _, columns = fcst_pert.shape
    column_blocks = lax.axis_size("mem")
    regions = lax.axis_size("dom")
    width = columns // column_blocks
    pair = local_members // regions
    grid = fcst_pert.reshape(leads, regions, pair, column_blocks, width)
    grid = jnp.transpose(grid, (3, 1, 0, 2, 4)).reshape(column_blocks * regions, -1)
    arrived = lax.all_to_all(grid, ("mem", "dom"), 0, 0, tiled=True)
    arrived = arrived.reshape(column_blocks, regions, leads, pair, width)
    targets = sensitivity.shape[1]
    levels = shifted_copies(sensitivity[:, :, 0, :], "dom")
    quarter = jnp.einsum("mdljc,dltc->mjlt", arrived, levels, precision=HIGH)
    quarter = quarter.reshape(column_blocks * pair, leads * targets)
    full = gathered(quarter, "dom").reshape(regions, column_blocks, pair, -1)
    summed = jnp.transpose(full, (1, 0, 2, 3)).reshape(column_blocks * local_members, -1)
    column_index = lax.axis_index("mem")
    region_index = lax.axis_index("dom")
    owned_rows = obs_pert.shape[0]
    owned_blocks = owned_rows // OBSB
    behind = from_behind(summed, "mem", 1)
    ahead = from_behind(summed, "mem", -1)
    weight_rows = own_weights(
        obs_lists, block_taper, counts, column_index, region_index, owned_blocks, regions
    )
    scale = (weighted_innovation / (M - 1))[:, None]
    rows = obs_pert * scale
    own = jnp.dot(rows, summed, precision=HIGH).reshape(owned_blocks, OBSB, -1)
    rows = rows.reshape(owned_blocks, OBSB, -1)
    others = weight_rows[0][:, None, None] * behind[None] + weight_rows[2][:, None, None] * ahead[None]
    result = own * weight_rows[1][:, None, None] + jnp.einsum(
        "irk,ikt->irt", rows, others, precision=HIGH
    )
    return result.reshape(owned_rows, -1)


def solution(mesh):
    in_specs = (
        P(None, "mem", "dom", None),
        P(None, None, "dom", "mem"),
        P(("mem", "dom"), None),
        P(("mem", "dom")),
        P(),
        P(),
        P(),
    )
    out_specs = P(("mem", "dom"), None)
    return jax.shard_map(body, mesh=mesh, in_specs=in_specs, out_specs=out_specs, check_vma=False)
```

```python
import jax
import jax.numpy as jnp
from jax import lax
from jax.sharding import PartitionSpec as P

M = 1024
OBSB = 128
HIGH = lax.Precision.HIGH


def from_behind(block, axis, distance):
    devices = range(lax.axis_size(axis))
    route = [((i - distance) % len(devices), i) for i in devices]
    return lax.ppermute(block, axis, route)


def gathered(piece, axis):
    count = lax.axis_size(axis)
    copies = jnp.broadcast_to(piece[None], (count,) + piece.shape)
    return lax.all_to_all(copies, axis, 0, 0, tiled=True)


def shifted_copies(piece, axis):
    count = lax.axis_size(axis)
    index = lax.axis_index(axis)
    arrived = [piece] + [from_behind(piece, axis, step) for step in range(1, count)]
    order = (index - jnp.arange(count, dtype=jnp.int32)) % count
    slots = jnp.zeros((count,) + piece.shape, piece.dtype)
    return slots.at[order].set(jnp.stack(arrived))


def own_weights(obs_lists, block_taper, counts, column_index, region_index, owned_blocks, regions):
    column_count, slots = obs_lists.shape
    rows = (column_index + jnp.arange(3, dtype=jnp.int32) - 1) % column_count
    row_ids = obs_lists[rows]
    row_taper = block_taper[rows]
    row_count = counts[rows]
    slot_live = jnp.arange(slots, dtype=jnp.int32)[None, :] < row_count[:, None]
    own_ids = (column_index * regions + region_index) * owned_blocks + jnp.arange(
        owned_blocks, dtype=jnp.int32
    )
    matched = (row_ids[:, None, :] == own_ids[None, :, None]) & slot_live[:, None, :]
    return jnp.sum(
        jnp.where(matched, row_taper[:, None, :], jnp.zeros((), row_taper.dtype)), axis=2
    )


def body(fcst_pert, sensitivity, obs_pert, weighted_innovation, obs_lists, block_taper, counts):
    leads, local_members, _, columns = fcst_pert.shape
    cores = lax.axis_size("core")
    column_blocks = lax.axis_size("pair") * cores
    regions = lax.axis_size("dom")
    width = columns // column_blocks
    pair = local_members // regions
    grid = fcst_pert.reshape(leads, regions, pair, column_blocks, width)
    grid = jnp.transpose(grid, (3, 1, 0, 2, 4)).reshape(column_blocks * regions, -1)
    arrived = lax.all_to_all(grid, ("pair", "core", "dom"), 0, 0, tiled=True)
    arrived = arrived.reshape(column_blocks, regions, leads, pair, width)
    targets = sensitivity.shape[1]
    levels = shifted_copies(sensitivity[:, :, 0, :], "dom")
    quarter = jnp.einsum("mdljc,dltc->mjlt", arrived, levels, precision=HIGH)
    quarter = quarter.reshape(column_blocks * pair, leads * targets)
    both = gathered(quarter, ("core", "dom")).reshape(cores, regions, column_blocks, pair, -1)
    both = jnp.transpose(both, (0, 2, 1, 3, 4)).reshape(cores, column_blocks * local_members, -1)
    core_index = lax.axis_index("core")
    column_index = lax.axis_index("pair") * cores + core_index
    region_index = lax.axis_index("dom")
    owned_rows = obs_pert.shape[0]
    owned_blocks = owned_rows // OBSB
    own = lax.dynamic_index_in_dim(both, core_index, 0, keepdims=False)
    partner = lax.dynamic_index_in_dim(both, 1 - core_index, 0, keepdims=False)
    route = [
        (i, (i + cores) % column_blocks if i % cores == 0 else (i - cores) % column_blocks)
        for i in range(column_blocks)
    ]
    far = lax.ppermute(partner, ("pair", "core"), route)
    weight_rows = own_weights(
        obs_lists, block_taper, counts, column_index, region_index, owned_blocks, regions
    )
    first = core_index == 0
    far_weight = jnp.where(first, weight_rows[0], weight_rows[2])
    partner_weight = jnp.where(first, weight_rows[2], weight_rows[0])
    scale = (weighted_innovation / (M - 1))[:, None]
    rows = obs_pert * scale
    rows = rows.reshape(owned_blocks, OBSB, -1)
    near = weight_rows[1][:, None, None] * own[None] + partner_weight[:, None, None] * partner[None]
    result = jnp.einsum("irk,ikt->irt", rows, near, precision=HIGH)
    distant = jnp.dot(rows.reshape(owned_rows, -1), far, precision=HIGH)
    result = result + distant.reshape(owned_blocks, OBSB, -1) * far_weight[:, None, None]
    return result.reshape(owned_rows, -1)


def solution(mesh):
    members, regions = mesh.devices.shape
    cores = 2
    split = jax.sharding.Mesh(
        mesh.devices.reshape(members // cores, cores, regions), ("pair", "core", "dom")
    )
    mem = ("pair", "core")
    in_specs = (
        P(None, mem, "dom", None),
        P(None, None, "dom", mem),
        P(mem + ("dom",), None),
        P(mem + ("dom",)),
        P(),
        P(),
        P(),
    )
    out_specs = P(mem + ("dom",), None)
    return jax.shard_map(body, mesh=split, in_specs=in_specs, out_specs=out_specs, check_vma=False)
```

```python
import jax
import jax.numpy as jnp
from jax import lax
from jax.sharding import PartitionSpec as P

M = 1024
OBSB = 128
HIGH = lax.Precision.HIGH


def from_behind(block, axis, distance):
    devices = range(lax.axis_size(axis))
    route = [((i - distance) % len(devices), i) for i in devices]
    return lax.ppermute(block, axis, route)


def gathered(piece, axis):
    count = lax.axis_size(axis)
    copies = jnp.broadcast_to(piece[None], (count,) + piece.shape)
    return lax.all_to_all(copies, axis, 0, 0, tiled=True)


def shifted_copies(piece, axis):
    count = lax.axis_size(axis)
    index = lax.axis_index(axis)
    arrived = [piece] + [from_behind(piece, axis, step) for step in range(1, count)]
    order = (index - jnp.arange(count, dtype=jnp.int32)) % count
    slots = jnp.zeros((count,) + piece.shape, piece.dtype)
    return slots.at[order].set(jnp.stack(arrived))


def own_weights(obs_lists, block_taper, counts, column_index, region_index, owned_blocks, regions):
    column_count, slots = obs_lists.shape
    rows = (column_index + jnp.arange(3, dtype=jnp.int32) - 1) % column_count
    row_ids = obs_lists[rows]
    row_taper = block_taper[rows]
    row_count = counts[rows]
    slot_live = jnp.arange(slots, dtype=jnp.int32)[None, :] < row_count[:, None]
    own_ids = (column_index * regions + region_index) * owned_blocks + jnp.arange(
        owned_blocks, dtype=jnp.int32
    )
    matched = (row_ids[:, None, :] == own_ids[None, :, None]) & slot_live[:, None, :]
    return jnp.sum(
        jnp.where(matched, row_taper[:, None, :], jnp.zeros((), row_taper.dtype)), axis=2
    )


def body(fcst_pert, sensitivity, obs_pert, weighted_innovation, obs_lists, block_taper, counts):
    leads, local_members, _, columns = fcst_pert.shape
    column_blocks = lax.axis_size("mem")
    regions = lax.axis_size("dom")
    width = columns // column_blocks
    pair = local_members // regions
    grid = fcst_pert.reshape(leads, regions, pair, column_blocks, width)
    grid = jnp.transpose(grid, (3, 1, 0, 2, 4)).reshape(column_blocks * regions, -1)
    arrived = lax.all_to_all(grid, ("mem", "dom"), 0, 0, tiled=True)
    arrived = arrived.reshape(column_blocks, regions, leads, pair, width)
    targets = sensitivity.shape[1]
    levels = shifted_copies(sensitivity[:, :, 0, :], "dom")
    quarter = jnp.einsum("mdljc,dltc->mjlt", arrived, levels, precision=HIGH)
    quarter = quarter.reshape(column_blocks * pair, leads * targets)
    full = gathered(quarter, "dom").reshape(regions, column_blocks, pair, -1)
    summed = jnp.transpose(full, (1, 0, 2, 3)).reshape(column_blocks * local_members, -1)
    column_index = lax.axis_index("mem")
    region_index = lax.axis_index("dom")
    owned_rows = obs_pert.shape[0]
    owned_blocks = owned_rows // OBSB
    behind = from_behind(summed, "mem", 1)
    ahead = from_behind(summed, "mem", -1)
    weight_rows = own_weights(
        obs_lists, block_taper, counts, column_index, region_index, owned_blocks, regions
    )
    scale = (weighted_innovation / (M - 1))[:, None]
    rows = obs_pert * scale
    result = 0
    for source, weights in zip((behind, summed, ahead), weight_rows):
        product = jnp.dot(rows, source, precision=HIGH).reshape(owned_blocks, OBSB, -1)
        result = result + product * weights[:, None, None]
    return result.reshape(owned_rows, -1)


def solution(mesh):
    in_specs = (
        P(None, "mem", "dom", None),
        P(None, None, "dom", "mem"),
        P(("mem", "dom"), None),
        P(("mem", "dom")),
        P(),
        P(),
        P(),
    )
    out_specs = P(("mem", "dom"), None)
    return jax.shard_map(body, mesh=mesh, in_specs=in_specs, out_specs=out_specs, check_vma=False)
```

```python
import jax
import jax.numpy as jnp
from jax import lax
from jax.sharding import PartitionSpec as P

M = 1024
OBSB = 128
HIGH = lax.Precision.HIGH


def from_behind(block, axis, distance):
    devices = range(lax.axis_size(axis))
    route = [((i - distance) % len(devices), i) for i in devices]
    return lax.ppermute(block, axis, route)


def gathered(piece, axis):
    count = lax.axis_size(axis)
    copies = jnp.broadcast_to(piece[None], (count,) + piece.shape)
    return lax.all_to_all(copies, axis, 0, 0, tiled=True)


def shifted_copies(piece, axis):
    count = lax.axis_size(axis)
    index = lax.axis_index(axis)
    arrived = [piece] + [from_behind(piece, axis, step) for step in range(1, count)]
    order = (index - jnp.arange(count, dtype=jnp.int32)) % count
    slots = jnp.zeros((count,) + piece.shape, piece.dtype)
    return slots.at[order].set(jnp.stack(arrived))


def own_weights(obs_lists, block_taper, counts, column_index, region_index, owned_blocks, regions):
    column_count, slots = obs_lists.shape
    rows = (column_index + jnp.arange(3, dtype=jnp.int32) - 1) % column_count
    row_ids = obs_lists[rows]
    row_taper = block_taper[rows]
    row_count = counts[rows]
    slot_live = jnp.arange(slots, dtype=jnp.int32)[None, :] < row_count[:, None]
    own_ids = (column_index * regions + region_index) * owned_blocks + jnp.arange(
        owned_blocks, dtype=jnp.int32
    )
    matched = (row_ids[:, None, :] == own_ids[None, :, None]) & slot_live[:, None, :]
    return jnp.sum(
        jnp.where(matched, row_taper[:, None, :], jnp.zeros((), row_taper.dtype)), axis=2
    )


def body(fcst_pert, sensitivity, obs_pert, weighted_innovation, obs_lists, block_taper, counts):
    leads, local_members, _, columns = fcst_pert.shape
    column_blocks = lax.axis_size("mem")
    regions = lax.axis_size("dom")
    width = columns // column_blocks
    pair = local_members // regions
    grid = fcst_pert.reshape(leads, regions, pair, column_blocks, width)
    grid = jnp.transpose(grid, (3, 1, 0, 2, 4)).reshape(column_blocks * regions, -1)
    arrived = lax.all_to_all(grid, ("mem", "dom"), 0, 0, tiled=True)
    arrived = arrived.reshape(column_blocks, regions, leads, pair, width)
    targets = sensitivity.shape[1]
    levels = shifted_copies(sensitivity[:, :, 0, :], "dom")
    quarter = jnp.einsum("mdljc,dltc->mjlt", arrived, levels, precision=HIGH)
    quarter = quarter.reshape(column_blocks * pair, leads * targets)
    summed = gathered(quarter, "dom").reshape(column_blocks * local_members, -1)
    column_index = lax.axis_index("mem")
    region_index = lax.axis_index("dom")
    owned_rows = obs_pert.shape[0]
    owned_blocks = owned_rows // OBSB
    behind = from_behind(summed, "mem", 1)
    ahead = from_behind(summed, "mem", -1)
    weight_rows = own_weights(
        obs_lists, block_taper, counts, column_index, region_index, owned_blocks, regions
    )
    scale = (weighted_innovation / (M - 1))[:, None]
    rows = obs_pert.reshape(owned_rows, column_blocks, regions, pair)
    rows = jnp.transpose(rows, (0, 2, 1, 3)).reshape(owned_rows, -1) * scale
    result = 0
    for source, weights in zip((behind, summed, ahead), weight_rows):
        product = jnp.dot(rows, source, precision=HIGH).reshape(owned_blocks, OBSB, -1)
        result = result + product * weights[:, None, None]
    return result.reshape(owned_rows, -1)


def solution(mesh):
    in_specs = (
        P(None, "mem", "dom", None),
        P(None, None, "dom", "mem"),
        P(("mem", "dom"), None),
        P(("mem", "dom")),
        P(),
        P(),
        P(),
    )
    out_specs = P(("mem", "dom"), None)
    return jax.shard_map(body, mesh=mesh, in_specs=in_specs, out_specs=out_specs, check_vma=False)
```

```python
import jax
import jax.numpy as jnp
from jax import lax
from jax.sharding import PartitionSpec as P

M = 1024
OBSB = 128
HIGH = lax.Precision.HIGH


def from_behind(block, axis, distance):
    devices = range(lax.axis_size(axis))
    route = [((i - distance) % len(devices), i) for i in devices]
    return lax.ppermute(block, axis, route)


def gathered(piece, axis):
    count = lax.axis_size(axis)
    copies = jnp.broadcast_to(piece[None], (count,) + piece.shape)
    return lax.all_to_all(copies, axis, 0, 0, tiled=True)


def shifted_copies(piece, axis):
    count = lax.axis_size(axis)
    index = lax.axis_index(axis)
    arrived = [piece] + [from_behind(piece, axis, step) for step in range(1, count)]
    order = (index - jnp.arange(count, dtype=jnp.int32)) % count
    slots = jnp.zeros((count,) + piece.shape, piece.dtype)
    return slots.at[order].set(jnp.stack(arrived))


def own_weights(obs_lists, block_taper, counts, column_index, region_index, owned_blocks, regions):
    column_count, slots = obs_lists.shape
    rows = (column_index + jnp.arange(3, dtype=jnp.int32) - 1) % column_count
    row_ids = obs_lists[rows]
    row_taper = block_taper[rows]
    row_count = counts[rows]
    slot_live = jnp.arange(slots, dtype=jnp.int32)[None, :] < row_count[:, None]
    own_ids = (column_index * regions + region_index) * owned_blocks + jnp.arange(
        owned_blocks, dtype=jnp.int32
    )
    matched = (row_ids[:, None, :] == own_ids[None, :, None]) & slot_live[:, None, :]
    return jnp.sum(
        jnp.where(matched, row_taper[:, None, :], jnp.zeros((), row_taper.dtype)), axis=2
    )


def body(fcst_pert, sensitivity, obs_pert, weighted_innovation, obs_lists, block_taper, counts):
    leads, local_members, _, columns = fcst_pert.shape
    column_blocks = lax.axis_size("mem")
    regions = lax.axis_size("dom")
    width = columns // column_blocks
    pair = local_members // regions
    grid = fcst_pert.reshape(leads, regions, pair, column_blocks, width)
    grid = jnp.transpose(grid, (3, 1, 0, 2, 4)).reshape(column_blocks * regions, -1)
    arrived = lax.all_to_all(grid, ("mem", "dom"), 0, 0, tiled=True)
    arrived = arrived.reshape(column_blocks, regions, leads, pair, width)
    targets = sensitivity.shape[1]
    levels = shifted_copies(sensitivity[:, :, 0, :], "dom")
    quarter = jnp.einsum("mdljc,dltc->mjlt", arrived, levels, precision=HIGH)
    quarter = quarter.reshape(column_blocks * pair, leads * targets)
    full = gathered(quarter, "dom").reshape(regions, column_blocks, pair, -1)
    summed = jnp.transpose(full, (1, 0, 2, 3)).reshape(column_blocks * local_members, -1)
    column_index = lax.axis_index("mem")
    region_index = lax.axis_index("dom")
    owned_rows = obs_pert.shape[0]
    owned_blocks = owned_rows // OBSB
    behind = from_behind(summed, "mem", 1)
    weight_rows = own_weights(
        obs_lists, block_taper, counts, column_index, region_index, owned_blocks, regions
    )
    scale = (weighted_innovation / (M - 1))[:, None]
    rows = obs_pert * scale

    def weighted(source, weights):
        product = jnp.dot(rows, source, precision=HIGH).reshape(owned_blocks, OBSB, -1)
        return product * weights[:, None, None]

    result = weighted(summed, weight_rows[1])
    summed, result = lax.optimization_barrier((summed, result))
    ahead = from_behind(summed, "mem", -1)
    result = result + weighted(behind, weight_rows[0])
    result = result + weighted(ahead, weight_rows[2])
    return result.reshape(owned_rows, -1)


def solution(mesh):
    in_specs = (
        P(None, "mem", "dom", None),
        P(None, None, "dom", "mem"),
        P(("mem", "dom"), None),
        P(("mem", "dom")),
        P(),
        P(),
        P(),
    )
    out_specs = P(("mem", "dom"), None)
    return jax.shard_map(body, mesh=mesh, in_specs=in_specs, out_specs=out_specs, check_vma=False)
```

```python
import jax
import jax.numpy as jnp
from jax import lax
from jax.sharding import PartitionSpec as P

M = 1024
OBSB = 128
HIGH = lax.Precision.HIGH


def from_behind(block, axis, distance):
    devices = range(lax.axis_size(axis))
    route = [((i - distance) % len(devices), i) for i in devices]
    return lax.ppermute(block, axis, route)


def gathered(piece, axis):
    count = lax.axis_size(axis)
    copies = jnp.broadcast_to(piece[None], (count,) + piece.shape)
    return lax.all_to_all(copies, axis, 0, 0, tiled=True)


def shifted_copies(piece, axis):
    count = lax.axis_size(axis)
    index = lax.axis_index(axis)
    arrived = [piece] + [from_behind(piece, axis, step) for step in range(1, count)]
    order = (index - jnp.arange(count, dtype=jnp.int32)) % count
    slots = jnp.zeros((count,) + piece.shape, piece.dtype)
    return slots.at[order].set(jnp.stack(arrived))


def own_weights(obs_lists, block_taper, counts, column_index, region_index, owned_blocks, regions):
    column_count, slots = obs_lists.shape
    rows = (column_index + jnp.arange(3, dtype=jnp.int32) - 1) % column_count
    row_ids = obs_lists[rows]
    row_taper = block_taper[rows]
    row_count = counts[rows]
    slot_live = jnp.arange(slots, dtype=jnp.int32)[None, :] < row_count[:, None]
    own_ids = (column_index * regions + region_index) * owned_blocks + jnp.arange(
        owned_blocks, dtype=jnp.int32
    )
    matched = (row_ids[:, None, :] == own_ids[None, :, None]) & slot_live[:, None, :]
    return jnp.sum(
        jnp.where(matched, row_taper[:, None, :], jnp.zeros((), row_taper.dtype)), axis=2
    )


def body(fcst_pert, sensitivity, obs_pert, weighted_innovation, obs_lists, block_taper, counts):
    leads, local_members, _, columns = fcst_pert.shape
    column_blocks = lax.axis_size("mem")
    regions = lax.axis_size("dom")
    width = columns // column_blocks
    pair = local_members // regions
    grid = fcst_pert.reshape(leads, regions, pair, column_blocks, width)
    grid = jnp.transpose(grid, (1, 3, 0, 2, 4)).reshape(regions * column_blocks, -1)
    arrived = lax.all_to_all(grid, ("dom", "mem"), 0, 0, tiled=True)
    arrived = arrived.reshape(regions, column_blocks, leads, pair, width)
    targets = sensitivity.shape[1]
    levels = shifted_copies(sensitivity[:, :, 0, :], "dom")
    quarter = jnp.einsum("dmljc,dltc->mjlt", arrived, levels, precision=HIGH)
    quarter = quarter.reshape(column_blocks * pair, leads * targets)
    full = gathered(quarter, "dom").reshape(regions, column_blocks, pair, -1)
    summed = jnp.transpose(full, (1, 0, 2, 3)).reshape(column_blocks * local_members, -1)
    column_index = lax.axis_index("mem")
    region_index = lax.axis_index("dom")
    owned_rows = obs_pert.shape[0]
    owned_blocks = owned_rows // OBSB
    behind = from_behind(summed, "mem", 1)
    ahead = from_behind(summed, "mem", -1)
    weight_rows = own_weights(
        obs_lists, block_taper, counts, column_index, region_index, owned_blocks, regions
    )
    scale = (weighted_innovation / (M - 1))[:, None]
    rows = obs_pert * scale
    result = 0
    for source, weights in zip((behind, summed, ahead), weight_rows):
        product = jnp.dot(rows, source, precision=HIGH).reshape(owned_blocks, OBSB, -1)
        result = result + product * weights[:, None, None]
    return result.reshape(owned_rows, -1)


def solution(mesh):
    in_specs = (
        P(None, "mem", "dom", None),
        P(None, None, "dom", "mem"),
        P(("mem", "dom"), None),
        P(("mem", "dom")),
        P(),
        P(),
        P(),
    )
    out_specs = P(("mem", "dom"), None)
    return jax.shard_map(body, mesh=mesh, in_specs=in_specs, out_specs=out_specs, check_vma=False)
```

```python
import jax
import jax.numpy as jnp
from jax import lax
from jax.sharding import PartitionSpec as P

M = 1024
OBSB = 128
HIGH = lax.Precision.HIGH


def from_behind(block, axis, distance):
    devices = range(lax.axis_size(axis))
    route = [((i - distance) % len(devices), i) for i in devices]
    return lax.ppermute(block, axis, route)


def gathered(piece, axis):
    count = lax.axis_size(axis)
    copies = jnp.broadcast_to(piece[None], (count,) + piece.shape)
    return lax.all_to_all(copies, axis, 0, 0, tiled=True)


def shifted_copies(piece, axis):
    count = lax.axis_size(axis)
    index = lax.axis_index(axis)
    arrived = [piece] + [from_behind(piece, axis, step) for step in range(1, count)]
    order = (index - jnp.arange(count, dtype=jnp.int32)) % count
    slots = jnp.zeros((count,) + piece.shape, piece.dtype)
    return slots.at[order].set(jnp.stack(arrived))


def own_weights(obs_lists, block_taper, counts, column_index, region_index, owned_blocks, regions):
    column_count, slots = obs_lists.shape
    rows = (column_index + jnp.arange(3, dtype=jnp.int32) - 1) % column_count
    row_ids = obs_lists[rows]
    row_taper = block_taper[rows]
    row_count = counts[rows]
    slot_live = jnp.arange(slots, dtype=jnp.int32)[None, :] < row_count[:, None]
    own_ids = (column_index * regions + region_index) * owned_blocks + jnp.arange(
        owned_blocks, dtype=jnp.int32
    )
    matched = (row_ids[:, None, :] == own_ids[None, :, None]) & slot_live[:, None, :]
    return jnp.sum(
        jnp.where(matched, row_taper[:, None, :], jnp.zeros((), row_taper.dtype)), axis=2
    )


def body(fcst_pert, sensitivity, obs_pert, weighted_innovation, obs_lists, block_taper, counts):
    leads, local_members, _, columns = fcst_pert.shape
    column_blocks = lax.axis_size("mem")
    regions = lax.axis_size("dom")
    width = columns // column_blocks
    pair = local_members // regions
    grid = fcst_pert.reshape(leads, regions, pair, column_blocks, width)
    grid = jnp.transpose(grid, (3, 1, 0, 2, 4)).reshape(column_blocks * regions, -1)
    arrived = lax.all_to_all(grid, ("mem", "dom"), 0, 0, tiled=True)
    arrived = arrived.reshape(column_blocks, regions, leads, pair, width)
    targets = sensitivity.shape[1]
    levels = shifted_copies(sensitivity[:, :, 0, :], "dom")
    quarter = jnp.einsum("mdljc,dltc->mjlt", arrived, levels, precision=HIGH)
    quarter = quarter.reshape(column_blocks * pair, leads * targets)
    lanes = quarter.reshape(column_blocks, 1, -1)
    copies = jnp.broadcast_to(lanes, (column_blocks, regions, lanes.shape[2]))
    summed = lax.all_to_all(copies, "dom", 1, 1, tiled=True)
    summed = summed.reshape(column_blocks * local_members, -1)
    column_index = lax.axis_index("mem")
    region_index = lax.axis_index("dom")
    owned_rows = obs_pert.shape[0]
    owned_blocks = owned_rows // OBSB
    behind = from_behind(summed, "mem", 1)
    ahead = from_behind(summed, "mem", -1)
    weight_rows = own_weights(
        obs_lists, block_taper, counts, column_index, region_index, owned_blocks, regions
    )
    scale = (weighted_innovation / (M - 1))[:, None]
    rows = obs_pert * scale
    result = 0
    for source, weights in zip((behind, summed, ahead), weight_rows):
        product = jnp.dot(rows, source, precision=HIGH).reshape(owned_blocks, OBSB, -1)
        result = result + product * weights[:, None, None]
    return result.reshape(owned_rows, -1)


def solution(mesh):
    in_specs = (
        P(None, "mem", "dom", None),
        P(None, None, "dom", "mem"),
        P(("mem", "dom"), None),
        P(("mem", "dom")),
        P(),
        P(),
        P(),
    )
    out_specs = P(("mem", "dom"), None)
    return jax.shard_map(body, mesh=mesh, in_specs=in_specs, out_specs=out_specs, check_vma=False)
```

```python
import jax
import jax.numpy as jnp
from jax import lax
from jax.sharding import PartitionSpec as P

M = 1024
OBSB = 128
HIGH = lax.Precision.HIGH


def from_behind(block, axis, distance):
    devices = range(lax.axis_size(axis))
    route = [((i - distance) % len(devices), i) for i in devices]
    return lax.ppermute(block, axis, route)


def gathered(piece, axis):
    count = lax.axis_size(axis)
    copies = jnp.broadcast_to(piece[None], (count,) + piece.shape)
    return lax.all_to_all(copies, axis, 0, 0, tiled=True)


def shifted_copies(piece, axis):
    count = lax.axis_size(axis)
    index = lax.axis_index(axis)
    arrived = [piece] + [from_behind(piece, axis, step) for step in range(1, count)]
    order = (index - jnp.arange(count, dtype=jnp.int32)) % count
    slots = jnp.zeros((count,) + piece.shape, piece.dtype)
    return slots.at[order].set(jnp.stack(arrived))


def own_weights(obs_lists, block_taper, counts, column_index, region_index, owned_blocks, regions):
    column_count, slots = obs_lists.shape
    rows = (column_index + jnp.arange(3, dtype=jnp.int32) - 1) % column_count
    row_ids = obs_lists[rows]
    row_taper = block_taper[rows]
    row_count = counts[rows]
    slot_live = jnp.arange(slots, dtype=jnp.int32)[None, :] < row_count[:, None]
    own_ids = (column_index * regions + region_index) * owned_blocks + jnp.arange(
        owned_blocks, dtype=jnp.int32
    )
    matched = (row_ids[:, None, :] == own_ids[None, :, None]) & slot_live[:, None, :]
    return jnp.sum(
        jnp.where(matched, row_taper[:, None, :], jnp.zeros((), row_taper.dtype)), axis=2
    )


def body(fcst_pert, sensitivity, obs_pert, weighted_innovation, obs_lists, block_taper, counts):
    leads, local_members, _, columns = fcst_pert.shape
    column_blocks = lax.axis_size("mem")
    regions = lax.axis_size("dom")
    width = columns // column_blocks
    pair = local_members // regions
    grid = fcst_pert.reshape(leads, regions, pair, column_blocks, width)
    grid = jnp.transpose(grid, (3, 1, 0, 2, 4)).reshape(column_blocks * regions, -1)
    arrived = lax.all_to_all(grid, ("mem", "dom"), 0, 0, tiled=True)
    arrived = arrived.reshape(column_blocks, regions, leads, pair, width)
    targets = sensitivity.shape[1]
    levels = shifted_copies(sensitivity[:, :, 0, :], "dom")
    quarter = jnp.einsum("mdljc,dltc->mjlt", arrived, levels, precision=HIGH)
    quarter = quarter.reshape(column_blocks * pair, leads * targets)
    full = gathered(quarter, "dom").reshape(regions, column_blocks, pair, -1)
    summed = jnp.transpose(full, (1, 0, 2, 3)).reshape(column_blocks * local_members, -1)
    column_index = lax.axis_index("mem")
    region_index = lax.axis_index("dom")
    owned_rows = obs_pert.shape[0]
    owned_blocks = owned_rows // OBSB
    count = lax.axis_size("mem")
    swap = [(i, i + 1 if i % 2 == 0 else i - 1) for i in range(count)]
    cross = [(i, (i - 1) % count if i % 2 == 0 else (i + 1) % count) for i in range(count)]
    near = lax.ppermute(summed, "mem", swap)
    far = lax.ppermute(summed, "mem", cross)
    weight_rows = own_weights(
        obs_lists, block_taper, counts, column_index, region_index, owned_blocks, regions
    )
    even = column_index % 2 == 0
    behind, ahead = far, near
    weight_rows = (
        jnp.where(even, weight_rows[0], weight_rows[2]),
        weight_rows[1],
        jnp.where(even, weight_rows[2], weight_rows[0]),
    )
    scale = (weighted_innovation / (M - 1))[:, None]
    rows = obs_pert * scale
    result = 0
    for source, weights in zip((behind, summed, ahead), weight_rows):
        product = jnp.dot(rows, source, precision=HIGH).reshape(owned_blocks, OBSB, -1)
        result = result + product * weights[:, None, None]
    return result.reshape(owned_rows, -1)


def solution(mesh):
    in_specs = (
        P(None, "mem", "dom", None),
        P(None, None, "dom", "mem"),
        P(("mem", "dom"), None),
        P(("mem", "dom")),
        P(),
        P(),
        P(),
    )
    out_specs = P(("mem", "dom"), None)
    return jax.shard_map(body, mesh=mesh, in_specs=in_specs, out_specs=out_specs, check_vma=False)
```

```python
import jax
import jax.numpy as jnp
from jax import lax
from jax.sharding import PartitionSpec as P

M = 1024
OBSB = 128
HIGH = lax.Precision.HIGH


def from_behind(block, axis, distance):
    devices = range(lax.axis_size(axis))
    route = [((i - distance) % len(devices), i) for i in devices]
    return lax.ppermute(block, axis, route)


def gathered(piece, axis):
    count = lax.axis_size(axis)
    copies = jnp.broadcast_to(piece[None], (count,) + piece.shape)
    return lax.all_to_all(copies, axis, 0, 0, tiled=True)


def shifted_copies(piece, axis):
    count = lax.axis_size(axis)
    index = lax.axis_index(axis)
    arrived = [piece] + [from_behind(piece, axis, step) for step in range(1, count)]
    order = (index - jnp.arange(count, dtype=jnp.int32)) % count
    slots = jnp.zeros((count,) + piece.shape, piece.dtype)
    return slots.at[order].set(jnp.stack(arrived))


def own_weights(obs_lists, block_taper, counts, column_index, region_index, owned_blocks, regions):
    column_count, slots = obs_lists.shape
    rows = (column_index + jnp.arange(3, dtype=jnp.int32) - 1) % column_count
    row_ids = obs_lists[rows]
    row_taper = block_taper[rows]
    row_count = counts[rows]
    slot_live = jnp.arange(slots, dtype=jnp.int32)[None, :] < row_count[:, None]
    own_ids = (column_index * regions + region_index) * owned_blocks + jnp.arange(
        owned_blocks, dtype=jnp.int32
    )
    matched = (row_ids[:, None, :] == own_ids[None, :, None]) & slot_live[:, None, :]
    return jnp.sum(
        jnp.where(matched, row_taper[:, None, :], jnp.zeros((), row_taper.dtype)), axis=2
    )


def body(fcst_pert, sensitivity, obs_pert, weighted_innovation, obs_lists, block_taper, counts):
    leads, local_members, _, columns = fcst_pert.shape
    column_blocks = lax.axis_size("mem")
    regions = lax.axis_size("dom")
    width = columns // column_blocks
    pair = local_members // regions
    grid = fcst_pert.reshape(leads, regions, pair, column_blocks, width)
    grid = jnp.transpose(grid, (3, 1, 0, 2, 4)).reshape(column_blocks * regions, leads * pair, width)
    arrived = lax.all_to_all(grid, ("mem", "dom"), 0, 0, tiled=True)
    arrived = arrived.reshape(column_blocks, regions, leads, pair, width)
    targets = sensitivity.shape[1]
    levels = shifted_copies(sensitivity[:, :, 0, :], "dom")
    quarter = jnp.einsum("mdljc,dltc->mjlt", arrived, levels, precision=HIGH)
    quarter = quarter.reshape(column_blocks * pair, leads * targets)
    full = gathered(quarter, "dom").reshape(regions, column_blocks, pair, -1)
    summed = jnp.transpose(full, (1, 0, 2, 3)).reshape(column_blocks * local_members, -1)
    column_index = lax.axis_index("mem")
    region_index = lax.axis_index("dom")
    owned_rows = obs_pert.shape[0]
    owned_blocks = owned_rows // OBSB
    count = lax.axis_size("mem")
    swap = [(i, i + 1 if i % 2 == 0 else i - 1) for i in range(count)]
    cross = [(i, (i - 1) % count if i % 2 == 0 else (i + 1) % count) for i in range(count)]
    near = lax.ppermute(summed, "mem", swap)
    far = lax.ppermute(summed, "mem", cross)
    weight_rows = own_weights(
        obs_lists, block_taper, counts, column_index, region_index, owned_blocks, regions
    )
    even = column_index % 2 == 0
    behind, ahead = far, near
    weight_rows = (
        jnp.where(even, weight_rows[0], weight_rows[2]),
        weight_rows[1],
        jnp.where(even, weight_rows[2], weight_rows[0]),
    )
    scale = (weighted_innovation / (M - 1))[:, None]
    rows = obs_pert * scale
    result = 0
    for source, weights in zip((behind, summed, ahead), weight_rows):
        product = jnp.dot(rows, source, precision=HIGH).reshape(owned_blocks, OBSB, -1)
        result = result + product * weights[:, None, None]
    return result.reshape(owned_rows, -1)


def solution(mesh):
    in_specs = (
        P(None, "mem", "dom", None),
        P(None, None, "dom", "mem"),
        P(("mem", "dom"), None),
        P(("mem", "dom")),
        P(),
        P(),
        P(),
    )
    out_specs = P(("mem", "dom"), None)
    return jax.shard_map(body, mesh=mesh, in_specs=in_specs, out_specs=out_specs, check_vma=False)
```

```python
import jax
import jax.numpy as jnp
from jax import lax
from jax.sharding import PartitionSpec as P

M = 1024
OBSB = 128
HIGH = lax.Precision.HIGH


def from_behind(block, axis, distance):
    devices = range(lax.axis_size(axis))
    route = [((i - distance) % len(devices), i) for i in devices]
    return lax.ppermute(block, axis, route)


def gathered(piece, axis):
    count = lax.axis_size(axis)
    copies = jnp.broadcast_to(piece[None], (count,) + piece.shape)
    return lax.all_to_all(copies, axis, 0, 0, tiled=True)


def shifted_copies(piece, axis):
    count = lax.axis_size(axis)
    index = lax.axis_index(axis)
    arrived = [piece] + [from_behind(piece, axis, step) for step in range(1, count)]
    order = (index - jnp.arange(count, dtype=jnp.int32)) % count
    slots = jnp.zeros((count,) + piece.shape, piece.dtype)
    return slots.at[order].set(jnp.stack(arrived))


def own_weights(obs_lists, block_taper, counts, column_index, region_index, owned_blocks, regions):
    column_count, slots = obs_lists.shape
    rows = (column_index + jnp.arange(3, dtype=jnp.int32) - 1) % column_count
    row_ids = obs_lists[rows]
    row_taper = block_taper[rows]
    row_count = counts[rows]
    slot_live = jnp.arange(slots, dtype=jnp.int32)[None, :] < row_count[:, None]
    own_ids = (column_index * regions + region_index) * owned_blocks + jnp.arange(
        owned_blocks, dtype=jnp.int32
    )
    matched = (row_ids[:, None, :] == own_ids[None, :, None]) & slot_live[:, None, :]
    return jnp.sum(
        jnp.where(matched, row_taper[:, None, :], jnp.zeros((), row_taper.dtype)), axis=2
    )


def body(fcst_pert, sensitivity, obs_pert, weighted_innovation, obs_lists, block_taper, counts):
    leads, local_members, _, columns = fcst_pert.shape
    column_blocks = lax.axis_size("mem")
    regions = lax.axis_size("dom")
    width = columns // column_blocks
    pair = local_members // regions
    grid = fcst_pert.reshape(leads, regions, pair, column_blocks, width)
    grid = jnp.transpose(grid, (3, 1, 0, 2, 4)).reshape(column_blocks * regions, -1)
    arrived = lax.all_to_all(grid, ("mem", "dom"), 0, 0, tiled=True)
    arrived = arrived.reshape(column_blocks, regions, leads, pair, width)
    targets = sensitivity.shape[1]
    levels = shifted_copies(sensitivity[:, :, 0, :], "dom")
    quarter = jnp.einsum("mdljc,dltc->mjlt", arrived, levels, precision=HIGH)
    quarter = quarter.reshape(column_blocks * pair, leads * targets)
    full = gathered(quarter, "dom").reshape(regions, column_blocks, pair, -1)
    summed = jnp.transpose(full, (1, 0, 2, 3)).reshape(column_blocks * local_members, -1)
    column_index = lax.axis_index("mem")
    region_index = lax.axis_index("dom")
    owned_rows = obs_pert.shape[0]
    owned_blocks = owned_rows // OBSB
    count = lax.axis_size("mem")
    swap = [(i, i + 1 if i % 2 == 0 else i - 1) for i in range(count)]
    cross = [(i, (i - 1) % count if i % 2 == 0 else (i + 1) % count) for i in range(count)]
    far = lax.ppermute(summed, "mem", cross)
    near = lax.ppermute(summed, "mem", swap)
    weight_rows = own_weights(
        obs_lists, block_taper, counts, column_index, region_index, owned_blocks, regions
    )
    even = column_index % 2 == 0
    behind, ahead = far, near
    weight_rows = (
        jnp.where(even, weight_rows[0], weight_rows[2]),
        weight_rows[1],
        jnp.where(even, weight_rows[2], weight_rows[0]),
    )
    scale = (weighted_innovation / (M - 1))[:, None]
    rows = obs_pert * scale
    result = 0
    for source, weights in zip((behind, summed, ahead), weight_rows):
        product = jnp.dot(rows, source, precision=HIGH).reshape(owned_blocks, OBSB, -1)
        result = result + product * weights[:, None, None]
    return result.reshape(owned_rows, -1)


def solution(mesh):
    in_specs = (
        P(None, "mem", "dom", None),
        P(None, None, "dom", "mem"),
        P(("mem", "dom"), None),
        P(("mem", "dom")),
        P(),
        P(),
        P(),
    )
    out_specs = P(("mem", "dom"), None)
    return jax.shard_map(body, mesh=mesh, in_specs=in_specs, out_specs=out_specs, check_vma=False)
```

```python
import jax
import jax.numpy as jnp
from jax import lax
from jax.sharding import PartitionSpec as P

M = 1024
OBSB = 128
HIGH = lax.Precision.HIGH


def from_behind(block, axis, distance):
    devices = range(lax.axis_size(axis))
    route = [((i - distance) % len(devices), i) for i in devices]
    return lax.ppermute(block, axis, route)


def gathered(piece, axis):
    count = lax.axis_size(axis)
    copies = jnp.broadcast_to(piece[None], (count,) + piece.shape)
    return lax.all_to_all(copies, axis, 0, 0, tiled=True)


def shifted_copies(piece, axis):
    count = lax.axis_size(axis)
    index = lax.axis_index(axis)
    arrived = [piece] + [from_behind(piece, axis, step) for step in range(1, count)]
    order = (index - jnp.arange(count, dtype=jnp.int32)) % count
    slots = jnp.zeros((count,) + piece.shape, piece.dtype)
    return slots.at[order].set(jnp.stack(arrived))


def own_weights(obs_lists, block_taper, counts, column_index, region_index, owned_blocks, regions):
    column_count, slots = obs_lists.shape
    rows = (column_index + jnp.arange(3, dtype=jnp.int32) - 1) % column_count
    row_ids = obs_lists[rows]
    row_taper = block_taper[rows]
    row_count = counts[rows]
    slot_live = jnp.arange(slots, dtype=jnp.int32)[None, :] < row_count[:, None]
    own_ids = (column_index * regions + region_index) * owned_blocks + jnp.arange(
        owned_blocks, dtype=jnp.int32
    )
    matched = (row_ids[:, None, :] == own_ids[None, :, None]) & slot_live[:, None, :]
    return jnp.sum(
        jnp.where(matched, row_taper[:, None, :], jnp.zeros((), row_taper.dtype)), axis=2
    )


def body(fcst_pert, sensitivity, obs_pert, weighted_innovation, obs_lists, block_taper, counts):
    leads, local_members, _, columns = fcst_pert.shape
    column_blocks = lax.axis_size("mem")
    regions = lax.axis_size("dom")
    width = columns // column_blocks
    pair = local_members // regions
    grid = fcst_pert.reshape(leads, regions, pair, column_blocks, width)
    grid = jnp.transpose(grid, (3, 1, 0, 2, 4)).reshape(column_blocks * regions, -1)
    arrived = lax.all_to_all(grid, ("mem", "dom"), 0, 0, tiled=True)
    arrived = arrived.reshape(column_blocks, regions, leads, pair, width)
    targets = sensitivity.shape[1]
    levels = shifted_copies(sensitivity[:, :, 0, :], "dom")
    quarter = jnp.einsum("mdljc,dltc->mjlt", arrived, levels, precision=HIGH)
    quarter = quarter.reshape(column_blocks * pair, leads * targets)
    full = gathered(quarter, "dom").reshape(regions, column_blocks, pair, -1)
    summed = jnp.transpose(full, (1, 0, 2, 3)).reshape(column_blocks * local_members, -1)
    column_index = lax.axis_index("mem")
    region_index = lax.axis_index("dom")
    owned_rows = obs_pert.shape[0]
    owned_blocks = owned_rows // OBSB
    count = lax.axis_size("mem")
    swap = [(i, i + 1 if i % 2 == 0 else i - 1) for i in range(count)]
    cross = [(i, (i - 1) % count if i % 2 == 0 else (i + 1) % count) for i in range(count)]
    far = lax.ppermute(summed, "mem", cross)
    near = lax.ppermute(summed, "mem", swap)
    weight_rows = own_weights(
        obs_lists, block_taper, counts, column_index, region_index, owned_blocks, regions
    )
    even = column_index % 2 == 0
    behind, ahead = far, near
    weight_rows = (
        jnp.where(even, weight_rows[0], weight_rows[2]),
        weight_rows[1],
        jnp.where(even, weight_rows[2], weight_rows[0]),
    )
    scale = (weighted_innovation / (M - 1))[:, None]
    rows = obs_pert * scale
    own = jnp.dot(rows, summed, precision=HIGH).reshape(owned_blocks, OBSB, -1)
    rows = rows.reshape(owned_blocks, OBSB, -1)
    others = weight_rows[0][:, None, None] * behind[None] + weight_rows[2][:, None, None] * ahead[None]
    result = own * weight_rows[1][:, None, None] + jnp.einsum(
        "irk,ikt->irt", rows, others, precision=HIGH
    )
    return result.reshape(owned_rows, -1)


def solution(mesh):
    in_specs = (
        P(None, "mem", "dom", None),
        P(None, None, "dom", "mem"),
        P(("mem", "dom"), None),
        P(("mem", "dom")),
        P(),
        P(),
        P(),
    )
    out_specs = P(("mem", "dom"), None)
    return jax.shard_map(body, mesh=mesh, in_specs=in_specs, out_specs=out_specs, check_vma=False)
```

```python
import jax
import jax.numpy as jnp
from jax import lax
from jax.sharding import PartitionSpec as P

M = 1024
OBSB = 128
HIGH = lax.Precision.HIGH


def from_behind(block, axis, distance):
    devices = range(lax.axis_size(axis))
    route = [((i - distance) % len(devices), i) for i in devices]
    return lax.ppermute(block, axis, route)


def gathered(piece, axis):
    count = lax.axis_size(axis)
    copies = jnp.broadcast_to(piece[None], (count,) + piece.shape)
    return lax.all_to_all(copies, axis, 0, 0, tiled=True)


def shifted_copies(piece, axis):
    count = lax.axis_size(axis)
    index = lax.axis_index(axis)
    arrived = [piece] + [from_behind(piece, axis, step) for step in range(1, count)]
    order = (index - jnp.arange(count, dtype=jnp.int32)) % count
    slots = jnp.zeros((count,) + piece.shape, piece.dtype)
    return slots.at[order].set(jnp.stack(arrived))


def own_weights(obs_lists, block_taper, counts, column_index, region_index, owned_blocks, regions):
    column_count, slots = obs_lists.shape
    rows = (column_index + jnp.arange(3, dtype=jnp.int32) - 1) % column_count
    row_ids = obs_lists[rows]
    row_taper = block_taper[rows]
    row_count = counts[rows]
    slot_live = jnp.arange(slots, dtype=jnp.int32)[None, :] < row_count[:, None]
    own_ids = (column_index * regions + region_index) * owned_blocks + jnp.arange(
        owned_blocks, dtype=jnp.int32
    )
    matched = (row_ids[:, None, :] == own_ids[None, :, None]) & slot_live[:, None, :]
    return jnp.sum(
        jnp.where(matched, row_taper[:, None, :], jnp.zeros((), row_taper.dtype)), axis=2
    )


def body(fcst_pert, sensitivity, obs_pert, weighted_innovation, obs_lists, block_taper, counts):
    leads, local_members, _, columns = fcst_pert.shape
    column_blocks = lax.axis_size("mem")
    regions = lax.axis_size("dom")
    width = columns // column_blocks
    pair = local_members // regions
    grid = fcst_pert.reshape(leads, regions, pair, column_blocks, width)
    grid = jnp.transpose(grid, (3, 1, 2, 0, 4)).reshape(column_blocks * regions, -1)
    arrived = lax.all_to_all(grid, ("mem", "dom"), 0, 0, tiled=True)
    arrived = arrived.reshape(column_blocks, regions, pair, leads, width)
    targets = sensitivity.shape[1]
    levels = shifted_copies(sensitivity[:, :, 0, :], "dom")
    quarter = jnp.einsum("mdjlc,dltc->mjlt", arrived, levels, precision=HIGH)
    quarter = quarter.reshape(column_blocks * pair, leads * targets)
    full = gathered(quarter, "dom").reshape(regions, column_blocks, pair, -1)
    summed = jnp.transpose(full, (1, 0, 2, 3)).reshape(column_blocks * local_members, -1)
    column_index = lax.axis_index("mem")
    region_index = lax.axis_index("dom")
    owned_rows = obs_pert.shape[0]
    owned_blocks = owned_rows // OBSB
    count = lax.axis_size("mem")
    swap = [(i, i + 1 if i % 2 == 0 else i - 1) for i in range(count)]
    cross = [(i, (i - 1) % count if i % 2 == 0 else (i + 1) % count) for i in range(count)]
    far = lax.ppermute(summed, "mem", cross)
    near = lax.ppermute(summed, "mem", swap)
    weight_rows = own_weights(
        obs_lists, block_taper, counts, column_index, region_index, owned_blocks, regions
    )
    even = column_index % 2 == 0
    behind, ahead = far, near
    weight_rows = (
        jnp.where(even, weight_rows[0], weight_rows[2]),
        weight_rows[1],
        jnp.where(even, weight_rows[2], weight_rows[0]),
    )
    scale = (weighted_innovation / (M - 1))[:, None]
    rows = obs_pert * scale
    own = jnp.dot(rows, summed, precision=HIGH).reshape(owned_blocks, OBSB, -1)
    rows = rows.reshape(owned_blocks, OBSB, -1)
    others = weight_rows[0][:, None, None] * behind[None] + weight_rows[2][:, None, None] * ahead[None]
    result = own * weight_rows[1][:, None, None] + jnp.einsum(
        "irk,ikt->irt", rows, others, precision=HIGH
    )
    return result.reshape(owned_rows, -1)


def solution(mesh):
    in_specs = (
        P(None, "mem", "dom", None),
        P(None, None, "dom", "mem"),
        P(("mem", "dom"), None),
        P(("mem", "dom")),
        P(),
        P(),
        P(),
    )
    out_specs = P(("mem", "dom"), None)
    return jax.shard_map(body, mesh=mesh, in_specs=in_specs, out_specs=out_specs, check_vma=False)
```

```python
import jax
import jax.numpy as jnp
from jax import lax
from jax.sharding import PartitionSpec as P

M = 1024
OBSB = 128
HIGH = lax.Precision.HIGH


def from_behind(block, axis, distance):
    devices = range(lax.axis_size(axis))
    route = [((i - distance) % len(devices), i) for i in devices]
    return lax.ppermute(block, axis, route)


def gathered(piece, axis):
    count = lax.axis_size(axis)
    copies = jnp.broadcast_to(piece[None], (count,) + piece.shape)
    return lax.all_to_all(copies, axis, 0, 0, tiled=True)


def shifted_copies(piece, axis):
    count = lax.axis_size(axis)
    index = lax.axis_index(axis)
    arrived = [piece] + [from_behind(piece, axis, step) for step in range(1, count)]
    order = (index - jnp.arange(count, dtype=jnp.int32)) % count
    slots = jnp.zeros((count,) + piece.shape, piece.dtype)
    return slots.at[order].set(jnp.stack(arrived))


def own_weights(obs_lists, block_taper, counts, column_index, region_index, owned_blocks, regions):
    column_count, slots = obs_lists.shape
    rows = (column_index + jnp.arange(3, dtype=jnp.int32) - 1) % column_count
    row_ids = obs_lists[rows]
    row_taper = block_taper[rows]
    row_count = counts[rows]
    slot_live = jnp.arange(slots, dtype=jnp.int32)[None, :] < row_count[:, None]
    own_ids = (column_index * regions + region_index) * owned_blocks + jnp.arange(
        owned_blocks, dtype=jnp.int32
    )
    matched = (row_ids[:, None, :] == own_ids[None, :, None]) & slot_live[:, None, :]
    return jnp.sum(
        jnp.where(matched, row_taper[:, None, :], jnp.zeros((), row_taper.dtype)), axis=2
    )


def body(fcst_pert, sensitivity, obs_pert, weighted_innovation, obs_lists, block_taper, counts):
    leads, local_members, _, columns = fcst_pert.shape
    column_blocks = lax.axis_size("mem")
    regions = lax.axis_size("dom")
    width = columns // column_blocks
    pair = local_members // regions
    grid = fcst_pert.reshape(leads, regions, pair, column_blocks, width)
    grid = jnp.transpose(grid, (3, 1, 2, 0, 4)).reshape(column_blocks * regions, -1)
    arrived = lax.all_to_all(grid, ("mem", "dom"), 0, 0, tiled=True)
    arrived = arrived.reshape(column_blocks, regions, pair, leads, width)
    targets = sensitivity.shape[1]
    levels = shifted_copies(sensitivity[:, :, 0, :], "dom")
    rows = obs_pert * (weighted_innovation / (M - 1))[:, None]
    levels, rows = lax.optimization_barrier((levels, rows))
    quarter = jnp.einsum("mdjlc,dltc->mjlt", arrived, levels, precision=HIGH)
    quarter = quarter.reshape(column_blocks * pair, leads * targets)
    full = gathered(quarter, "dom").reshape(regions, column_blocks, pair, -1)
    summed = jnp.transpose(full, (1, 0, 2, 3)).reshape(column_blocks * local_members, -1)
    column_index = lax.axis_index("mem")
    region_index = lax.axis_index("dom")
    owned_rows = obs_pert.shape[0]
    owned_blocks = owned_rows // OBSB
    count = lax.axis_size("mem")
    swap = [(i, i + 1 if i % 2 == 0 else i - 1) for i in range(count)]
    cross = [(i, (i - 1) % count if i % 2 == 0 else (i + 1) % count) for i in range(count)]
    far = lax.ppermute(summed, "mem", cross)
    near = lax.ppermute(summed, "mem", swap)
    weight_rows = own_weights(
        obs_lists, block_taper, counts, column_index, region_index, owned_blocks, regions
    )
    even = column_index % 2 == 0
    behind, ahead = far, near
    weight_rows = (
        jnp.where(even, weight_rows[0], weight_rows[2]),
        weight_rows[1],
        jnp.where(even, weight_rows[2], weight_rows[0]),
    )
    own = jnp.dot(rows, summed, precision=HIGH).reshape(owned_blocks, OBSB, -1)
    rows = rows.reshape(owned_blocks, OBSB, -1)
    others = weight_rows[0][:, None, None] * behind[None] + weight_rows[2][:, None, None] * ahead[None]
    result = own * weight_rows[1][:, None, None] + jnp.einsum(
        "irk,ikt->irt", rows, others, precision=HIGH
    )
    return result.reshape(owned_rows, -1)


def solution(mesh):
    in_specs = (
        P(None, "mem", "dom", None),
        P(None, None, "dom", "mem"),
        P(("mem", "dom"), None),
        P(("mem", "dom")),
        P(),
        P(),
        P(),
    )
    out_specs = P(("mem", "dom"), None)
    return jax.shard_map(body, mesh=mesh, in_specs=in_specs, out_specs=out_specs, check_vma=False)
```
